512 devices in a mesh: row: 16 (over x, y), col: 32 (over z, core).
Axes of the slice: x: 4, y: 4, z: 16, core: 2. Of those that a mesh axis runs over, the one named last changes fastest.
Arguments:
- observed: int32 [32, 3072, 2048], P('col', 'row'), may hold values from 0 to 1, as said below
- user_effect: float32 [32, 3072], P('col', 'row'), may hold values from -4 to 4
- item_effect: float32 [128, 128], replicated, may hold values from -4 to 4
- block_list: int32 [32, 16], replicated, may hold values from 0 to 127, as said below
Outputs:
- factored: float32 [8, 16, 128, 4, 32, 128], P(None, 'row', None, None, 'col')
- correction: bfloat16 [8, 16, 128, 4, 32, 128], P(None, 'row', None, None, 'col')
- logdet: float32 [], replicated
- pivots: float32 [16, 32, 32], P('row', 'col')
The draws below stay inside these ranges and needn't reach their ends.
Inputs may be any that keep to these rules, and one draw needn't show every extreme that they name: `block_list`: each row lists 16 distinct tiles; entry k has remainder k // (16 // 16) modulo 16; at most max(1, 16 // 32) entries of a row share a remainder modulo 32, and some remainder reaches that count in every row. `observed`: 1 marks a rating of the user for the item.
All inputs are finite; a program needn't handle non-finite values.
Results may differ from the reference program's by a relative error of at most 0.0069.
Values may be sent and summed in bfloat16 or wider, within the bound.
No kernel may reach another device: no remote copies, remote signals or barrier semaphores. Data moves between devices by JAX's collectives and lax.ppermute only.
A program may use at most 128 MiB of HBM per device.

```python
import jax
import jax.numpy as jnp
from jax import lax

TILE = 128
ITEMS = 16384
K = 16
PANEL_BLOCKS = 2
U_DEV = 192
NB = 128
USERS = 3072
N_ROW = 16
N_COL = 32


def draw_observed(key, part):
    width = K * TILE
    keys = jax.random.split(jax.random.fold_in(key, 29), 4)
    activity = jax.random.randint(keys[0], (N_COL, USERS, 1), 0, 4)
    popularity = jax.random.randint(keys[1], (N_COL, 1, width), 0, 3)
    favored = jax.random.randint(keys[2], (N_COL, USERS, 1), 0, K)
    tile_of = (jnp.arange(width, dtype=jnp.int32) // TILE)[None, None, :]
    boost = jnp.where(tile_of == favored, 3, 0).astype(jnp.int32)
    rate = jnp.left_shift(jnp.ones((), jnp.int32), (activity + popularity + boost).astype(jnp.int32))
    rolled = jax.random.randint(keys[3], (N_COL, USERS, width), 0, 2 * width)
    return (rolled < rate).astype(jnp.int32)


def draw_block_list(key, part):
    per_row = K // N_ROW
    ratio = N_COL // N_ROW
    span = ITEMS // TILE // N_COL
    first, second = jax.random.split(jax.random.fold_in(key, 17))
    offset = jax.random.randint(first, (N_COL, N_ROW, 1), 0, ratio)
    within = jnp.arange(per_row, dtype=jnp.int32)[None, None, :]
    choice_m = (within + offset) % ratio
    residue = jnp.arange(N_ROW, dtype=jnp.int32)[None, :, None] + N_ROW * choice_m
    base = jax.random.randint(second, (N_COL, N_ROW, ratio), 0, span)
    picked = jnp.take_along_axis(base, choice_m, axis=2)
    level = (picked + within // ratio) % span
    blocks = residue + N_COL * level
    return blocks.reshape(N_COL, K).astype(jnp.int32)


def block_levels(rng, dims, pieces, least, largest):
    level, own = 1.0, jax.random.fold_in(rng, 6)
    for position, blocks in pieces:
        steps = jnp.exp(jax.random.uniform(jax.random.fold_in(own, position), (blocks,), jnp.float32, least / len(pieces), largest / len(pieces)))
        level = level * jnp.repeat(steps, dims[position] // blocks).reshape([-1 if axis == position else 1 for axis in range(len(dims))])
    return level


def scatter_about(rng, shape, spread, reach, cuts=(), kind=jnp.bfloat16):
    loudness = block_levels(rng, shape, cuts, -0.22, 0.18) if cuts else 1.0
    entries = jax.random.normal(rng, shape, jnp.float32) * spread * loudness
    return jnp.minimum(jnp.maximum(entries, -reach), reach).astype(kind)


def setup_inputs(seed: int = 0) -> dict:
    key_list = jax.random.split(jax.random.key(seed), 5)
    observed = draw_observed(jax.random.fold_in(key_list[4], 71), 0)
    user_effect = scatter_about(key_list[1], (N_COL, USERS), 1.0, 4.0, ((0, 32), (1, 16)), jnp.float32)
    item_effect = scatter_about(key_list[2], (NB, TILE), 1.0, 4.0, (), jnp.float32)
    block_list = draw_block_list(jax.random.fold_in(key_list[4], 71), 0)
    return dict(observed=observed, user_effect=user_effect, item_effect=item_effect, block_list=block_list)


highest = lax.Precision.HIGHEST
user_prior = 1.0
item_prior = 1.0

def reference(observed, user_effect, item_effect, block_list):
    width = K * TILE

    def cluster(index, schur):
        blocks = lax.dynamic_index_in_dim(block_list, index, 0, keepdims=False)
        marks = lax.dynamic_index_in_dim(observed, index, 0, keepdims=False)
        effects = lax.dynamic_index_in_dim(user_effect, index, 0, keepdims=False)
        picker = (blocks[:, None] == jnp.arange(NB, dtype=jnp.int32)[None, :]).astype(jnp.float32)
        item_vals = jnp.dot(picker, item_effect, precision=highest).reshape(width)
        prob = jax.nn.sigmoid(effects[:, None] + item_vals[None, :])
        weight = jnp.where(marks > 0, prob * (1.0 - prob), 0.0)
        precision_u = user_prior + lax.optimization_barrier(jnp.sum(weight, axis=1))
        scaled = (weight / jnp.sqrt(precision_u)[:, None]).astype(jnp.bfloat16)
        col_total = lax.optimization_barrier(jnp.sum(weight, axis=0))

        def device_part(total, group):
            part = lax.dynamic_slice_in_dim(scaled, group * U_DEV, U_DEV, 0).astype(jnp.float32)
            product = jnp.dot(part.T, part, precision=highest)
            rounded = lax.optimization_barrier(product.astype(jnp.bfloat16))
            return (total + rounded.astype(jnp.float32), None)
        cross, _ = lax.scan(device_part, jnp.zeros((width, width), jnp.float32), jnp.arange(N_ROW, dtype=jnp.int32))
        block = jnp.diag(col_total) - cross
        ids = (blocks[:, None] * TILE + jnp.arange(TILE, dtype=jnp.int32)[None, :]).reshape(width).astype(jnp.int32)
        return schur.at[ids[:, None], ids[None, :]].add(block)
    schur = lax.fori_loop(0, N_COL, cluster, jnp.zeros((ITEMS, ITEMS), jnp.float32))
    schur = schur + item_prior * jnp.eye(ITEMS, dtype=jnp.float32)
    width_p = PANEL_BLOCKS * TILE
    lower = jnp.linalg.cholesky(schur[:width_p, :width_p])
    factor = lax.linalg.triangular_solve(lower, schur[:, :width_p], left_side=False, lower=True, transpose_a=True)
    logdet = 2.0 * jnp.sum(jnp.log(jnp.diagonal(lower)))
    update = jnp.dot(factor, factor.T, precision=highest)
    positions = jnp.arange(ITEMS, dtype=jnp.int32)
    below = positions >= width_p
    trailing = jnp.where(below[:, None], schur - update, 0.0)
    full = trailing.at[:, :width_p].set(factor)
    diagonal_vals = jnp.diagonal(full)
    full = full.at[positions, positions].set(0.0)
    pivots = diagonal_vals.reshape(NB // N_COL, N_COL, TILE).transpose(1, 0, 2)
    pivots = pivots.reshape(N_COL, N_ROW, ITEMS // (N_ROW * N_COL)).transpose(1, 0, 2)
    correction = jnp.where(below[:, None] & below[None, :], update, 0.0).astype(jnp.bfloat16)
    shape_out = (NB // N_ROW, N_ROW, TILE, NB // N_COL, N_COL, TILE)
    return (full.reshape(shape_out), correction.reshape(shape_out), logdet, pivots)
```

```python
import jax
import jax.numpy as jnp
from jax import lax
from jax.sharding import PartitionSpec as P

PANEL_BLOCKS = 2


highest = lax.Precision.HIGHEST
user_prior = 1.0
item_prior = 1.0


def body(observed, user_effect, item_effect, block_list):
    rows_n = lax.axis_size("row")
    cols_n = lax.axis_size("col")
    row_idx = lax.axis_index("row")
    col_idx = lax.axis_index("col")
    nblocks, tile = item_effect.shape
    kcount = block_list.shape[1]
    per_row = kcount // rows_n
    slots = max(1, kcount // cols_n)
    width = kcount * tile
    group = per_row * tile
    nb_r = nblocks // rows_n
    nb_c = nblocks // cols_n
    width_p = PANEL_BLOCKS * tile
    mine = lax.dynamic_index_in_dim(block_list, col_idx, 0, keepdims=False)
    picker = (mine[:, None] == jnp.arange(nblocks)[None, :]).astype(jnp.float32)
    item_vals = jnp.dot(picker, item_effect, precision=highest).reshape(width)
    marks = observed[0]
    prob = jax.nn.sigmoid(user_effect[0][:, None] + item_vals[None, :])
    weight = jnp.where(marks > 0, prob * (1.0 - prob), 0.0)
    precision_u = user_prior + jnp.sum(weight, axis=1)
    scaled = (weight / jnp.sqrt(precision_u)[:, None]).astype(jnp.bfloat16)
    col_share = lax.psum_scatter(jnp.sum(weight, axis=0), "row", scatter_dimension=0, tiled=True)

    product = lax.dot_general(
        scaled, scaled, (((0,), (0,)), ((), ())), preferred_element_type=jnp.float32
    ).astype(jnp.bfloat16)
    grouped = product.reshape(rows_n, group, width)
    arrived = lax.all_to_all(grouped, "row", split_axis=0, concat_axis=0, tiled=True)
    cross = jnp.sum(arrived, axis=0, dtype=jnp.float32)
    global_rows = row_idx * group + jnp.arange(group)
    diag_part = jnp.where(
        global_rows[:, None] == jnp.arange(width)[None, :], col_share[:, None], 0.0
    )
    strip = (diag_part - cross).reshape(per_row, tile, kcount, tile)
    row_block = lax.dynamic_slice_in_dim(mine, row_idx * per_row, per_row, 0)

    holds = mine[None, :] == jnp.arange(PANEL_BLOCKS)[:, None]
    panel_part = jnp.sum(
        jnp.where(holds[None, None, :, :, None], strip[:, :, None, :, :], 0.0), axis=3
    )
    at_row = (row_block[:, None] // rows_n) == jnp.arange(nb_r)[None, :]
    placed = jnp.sum(
        jnp.where(at_row[:, :, None, None, None], panel_part[:, None], 0.0), axis=0
    )
    row_ids = jnp.arange(nb_r) * rows_n + row_idx
    col_ids = jnp.arange(nb_c) * cols_n + col_idx
    eye = jnp.eye(tile, dtype=jnp.float32)
    panel_eye = jnp.where(
        (row_ids[:, None] == jnp.arange(PANEL_BLOCKS)[None, :])[:, None, :, None],
        item_prior * eye[None, :, None, :],
        0.0,
    )
    panel = lax.psum(placed, "col") + panel_eye

    residue = block_list % cols_n
    same = residue[:, :, None] == residue[:, None, :]
    before = jnp.arange(kcount)[None, :] < jnp.arange(kcount)[:, None]
    rank = jnp.sum((same & before[None]).astype(jnp.int32), axis=2)
    my_res = lax.dynamic_index_in_dim(residue, col_idx, 0, keepdims=False)
    my_rank = lax.dynamic_index_in_dim(rank, col_idx, 0, keepdims=False)
    chooser = (
        (my_res[None, None, :] == jnp.arange(cols_n)[:, None, None])
        & (my_rank[None, None, :] == jnp.arange(slots)[None, :, None])
    ).astype(jnp.float32)
    outgoing = jnp.einsum("csk,jakb->csjab", chooser, strip, precision=highest)
    incoming = lax.all_to_all(outgoing, "col", split_axis=0, concat_axis=0, tiled=True)
    picks = (residue == col_idx)[:, None, :] & (
        rank[:, None, :] == jnp.arange(slots)[None, :, None]
    )
    col_block = jnp.sum(jnp.where(picks, block_list[:, None, :], 0), axis=2)
    valid = jnp.any(picks, axis=2)
    row_blocks = lax.dynamic_slice_in_dim(block_list, row_idx * per_row, per_row, 1)
    sel = (
        valid[:, :, None, None, None]
        & ((row_blocks[:, None, :] // rows_n)[:, :, :, None, None] == jnp.arange(nb_r)[None, None, None, :, None])
        & ((col_block[:, :, None] // cols_n)[:, :, :, None, None] == jnp.arange(nb_c)[None, None, None, None, :])
    )
    on_diag = row_ids[:, None] == col_ids[None, :]
    tiles = jnp.einsum(
        "cvjiq,cvjst->isqt",
        sel.astype(jnp.float32),
        incoming,
        precision=highest,
    )
    schur = tiles + jnp.where(on_diag[:, None, :, None], item_prior * eye[None, :, None, :], 0.0)

    top = (row_idx < PANEL_BLOCKS).astype(jnp.float32)
    first = (jnp.arange(PANEL_BLOCKS) == row_idx).astype(jnp.float32)
    col_panel = schur[0].transpose(1, 0, 2)[:, None] * first[None, :, None, None]
    corner_part = panel[0][None] * first[:, None, None, None] * top
    diag_tile = jnp.diagonal(schur, axis1=1, axis2=3)
    diag_vals = jnp.sum(jnp.where(on_diag[:, :, None], diag_tile, 0.0), axis=0)
    sizes = (col_panel.size, corner_part.size, diag_vals.size)
    packed = jnp.concatenate(
        [col_panel.reshape(-1), corner_part.reshape(-1), diag_vals.reshape(-1)]
    )
    shared = lax.psum(packed, "row")
    col_panel = shared[: sizes[0]].reshape(nb_c, PANEL_BLOCKS, tile, tile)
    corner = shared[sizes[0] : sizes[0] + sizes[1]].reshape(width_p, width_p)
    col_diag = shared[sizes[0] + sizes[1] :].reshape(nb_c, tile)

    lower = jnp.linalg.cholesky(corner)
    logdet = 2.0 * jnp.sum(jnp.log(jnp.diagonal(lower)))
    panel_cols = col_panel.transpose(0, 3, 1, 2).reshape(nb_c * tile, width_p)
    rhs = jnp.concatenate([panel.reshape(nb_r * tile, width_p), panel_cols], axis=0)
    solved = lax.linalg.triangular_solve(
        lower, rhs, left_side=False, lower=True, transpose_a=True
    )
    factor_rows = solved[: nb_r * tile].reshape(nb_r, tile, width_p)
    factor_cols = solved[nb_r * tile :].reshape(nb_c, tile, width_p)
    update = jnp.einsum("isk,jtk->isjt", factor_rows, factor_cols, precision=highest)
    own_panel = lax.dynamic_slice_in_dim(
        factor_rows, jnp.minimum(col_idx, PANEL_BLOCKS - 1) * tile, tile, 2
    )
    in_panel = col_ids < PANEL_BLOCKS
    above = row_ids < PANEL_BLOCKS
    trailing = jnp.where(above[:, None, None, None], 0.0, schur - update)
    result = jnp.where(in_panel[None, None, :, None], own_panel[:, :, None, :], trailing)
    diag_entry = on_diag[:, None, :, None] & eye.astype(bool)[None, :, None, :]
    cleared = jnp.where(diag_entry, 0.0, result)
    factored = cleared[:, None, :, :, None, :]
    trailing_mask = (
        jnp.logical_not(above)[:, None, None, None] & jnp.logical_not(in_panel)[None, None, :, None]
    )
    rounded_update = jnp.where(trailing_mask, update, 0.0).astype(jnp.bfloat16)
    corrected = rounded_update[:, None, :, :, None, :]

    share = nblocks * tile // (rows_n * cols_n)
    start = row_idx * share
    piv_jj = start // tile
    piv_s = start % tile
    piv_block = piv_jj * cols_n + col_idx
    piv_rows = lax.dynamic_slice_in_dim(
        lax.dynamic_index_in_dim(factor_cols, piv_jj, 0, keepdims=False), piv_s, share, 0
    )
    piv_diag = lax.dynamic_slice_in_dim(
        lax.dynamic_index_in_dim(col_diag, piv_jj, 0, keepdims=False), piv_s, share, 0
    )
    trail_piv = piv_diag - jnp.sum(piv_rows * piv_rows, axis=1)
    panel_at = piv_block * tile + piv_s + jnp.arange(share)
    panel_piv = jnp.sum(
        jnp.where(panel_at[:, None] == jnp.arange(width_p)[None, :], piv_rows, 0.0), axis=1
    )
    piv = jnp.where(piv_block < PANEL_BLOCKS, panel_piv, trail_piv)
    pivots = piv.reshape(1, 1, share)
    return (factored, corrected, logdet, pivots)


def solution(mesh):
    in_specs = (P("col", "row", None), P("col", "row"), P(), P())
    out_specs = (
        P(None, "row", None, None, "col", None),
        P(None, "row", None, None, "col", None),
        P(),
        P("row", "col", None),
    )
    return jax.shard_map(body, mesh=mesh, in_specs=in_specs, out_specs=out_specs, check_vma=False)
```

```python
import jax
import jax.numpy as jnp
from jax import lax
from jax.sharding import PartitionSpec as P

PANEL_BLOCKS = 2


highest = lax.Precision.HIGHEST
user_prior = 1.0
item_prior = 1.0


def spread_sum(flat, axis, count):
    size = flat.shape[0]
    unit = count * 1024
    padded = -(-size // unit) * unit
    flat = jnp.pad(flat, (0, padded - size))
    got = lax.all_to_all(flat.reshape(count, padded // count), axis, 0, 0, tiled=True)
    part = jnp.sum(got, axis=0)
    spread = jnp.broadcast_to(part[None], (count, padded // count))
    out = lax.all_to_all(spread, axis, 0, 0, tiled=True)
    return out.reshape(padded)[:size]


def body(observed, user_effect, item_effect, block_list):
    rows_n = lax.axis_size("row")
    cols_n = lax.axis_size("col")
    row_idx = lax.axis_index("row")
    col_idx = lax.axis_index("col")
    nblocks, tile = item_effect.shape
    kcount = block_list.shape[1]
    per_row = kcount // rows_n
    slots = max(1, kcount // cols_n)
    width = kcount * tile
    group = per_row * tile
    nb_r = nblocks // rows_n
    nb_c = nblocks // cols_n
    width_p = PANEL_BLOCKS * tile
    mine = lax.dynamic_index_in_dim(block_list, col_idx, 0, keepdims=False)
    picker = (mine[:, None] == jnp.arange(nblocks)[None, :]).astype(jnp.float32)
    item_vals = jnp.dot(picker, item_effect, precision=highest).reshape(width)
    marks = observed[0]
    prob = jax.nn.sigmoid(user_effect[0][:, None] + item_vals[None, :])
    weight = jnp.where(marks > 0, prob * (1.0 - prob), 0.0)
    precision_u = user_prior + jnp.sum(weight, axis=1)
    scaled = (weight / jnp.sqrt(precision_u)[:, None]).astype(jnp.bfloat16)
    col_share = lax.psum_scatter(jnp.sum(weight, axis=0), "row", scatter_dimension=0, tiled=True)

    product = lax.dot_general(
        scaled, scaled, (((0,), (0,)), ((), ())), preferred_element_type=jnp.float32
    ).astype(jnp.bfloat16)
    grouped = product.reshape(rows_n, group, width)
    arrived = lax.all_to_all(grouped, "row", split_axis=0, concat_axis=0, tiled=True)
    cross = jnp.sum(arrived, axis=0, dtype=jnp.float32)
    global_rows = row_idx * group + jnp.arange(group)
    diag_part = jnp.where(
        global_rows[:, None] == jnp.arange(width)[None, :], col_share[:, None], 0.0
    )
    strip = (diag_part - cross).reshape(per_row, tile, kcount, tile)

    holds = mine[None, :] == jnp.arange(PANEL_BLOCKS)[:, None]
    panel_part = jnp.sum(
        jnp.where(holds[None, None, :, :, None], strip[:, :, None, :, :], 0.0), axis=3
    )
    row_ids = jnp.arange(nb_r) * rows_n + row_idx
    col_ids = jnp.arange(nb_c) * cols_n + col_idx
    eye = jnp.eye(tile, dtype=jnp.float32)
    panel_eye = jnp.where(
        (row_ids[:, None] == jnp.arange(PANEL_BLOCKS)[None, :])[:, None, :, None],
        item_prior * eye[None, :, None, :],
        0.0,
    )
    piece = tile // cols_n
    contrib = panel_part.reshape(per_row, cols_n, piece, width_p).transpose(1, 0, 2, 3)
    gathered = lax.all_to_all(contrib, "col", 0, 0, tiled=True)
    row_blocks_all = lax.dynamic_slice_in_dim(block_list, row_idx * per_row, per_row, 1)
    slot_of = (row_blocks_all // rows_n)[:, :, None] == jnp.arange(nb_r)[None, None, :]
    part = jnp.sum(
        jnp.where(slot_of[:, :, :, None, None], gathered[:, :, None], 0.0), axis=(0, 1)
    )
    spread = jnp.broadcast_to(part[None], (cols_n, nb_r, piece, width_p))
    pieces = lax.all_to_all(spread, "col", 0, 0, tiled=True)
    panel = pieces.transpose(1, 0, 2, 3).reshape(nb_r, tile, PANEL_BLOCKS, tile) + panel_eye

    residue = block_list % cols_n
    same = residue[:, :, None] == residue[:, None, :]
    before = jnp.arange(kcount)[None, :] < jnp.arange(kcount)[:, None]
    rank = jnp.sum((same & before[None]).astype(jnp.int32), axis=2)
    my_res = lax.dynamic_index_in_dim(residue, col_idx, 0, keepdims=False)
    my_rank = lax.dynamic_index_in_dim(rank, col_idx, 0, keepdims=False)
    chooser = (
        (my_res[None, None, :] == jnp.arange(cols_n)[:, None, None])
        & (my_rank[None, None, :] == jnp.arange(slots)[None, :, None])
    ).astype(jnp.float32)
    outgoing = jnp.einsum("csk,jakb->csjab", chooser, strip, precision=highest)
    incoming = lax.all_to_all(
        outgoing.astype(jnp.bfloat16), "col", split_axis=0, concat_axis=0, tiled=True
    ).astype(jnp.float32)
    picks = (residue == col_idx)[:, None, :] & (
        rank[:, None, :] == jnp.arange(slots)[None, :, None]
    )
    col_block = jnp.sum(jnp.where(picks, block_list[:, None, :], 0), axis=2)
    valid = jnp.any(picks, axis=2)
    row_blocks = lax.dynamic_slice_in_dim(block_list, row_idx * per_row, per_row, 1)
    sel = (
        valid[:, :, None, None, None]
        & ((row_blocks[:, None, :] // rows_n)[:, :, :, None, None] == jnp.arange(nb_r)[None, None, None, :, None])
        & ((col_block[:, :, None] // cols_n)[:, :, :, None, None] == jnp.arange(nb_c)[None, None, None, None, :])
    )
    on_diag = row_ids[:, None] == col_ids[None, :]
    tiles = jnp.einsum(
        "cvjiq,cvjst->isqt",
        sel.astype(jnp.float32),
        incoming,
        precision=highest,
    )
    schur = tiles + jnp.where(on_diag[:, None, :, None], item_prior * eye[None, :, None, :], 0.0)

    top = (row_idx < PANEL_BLOCKS).astype(jnp.float32)
    first = (jnp.arange(PANEL_BLOCKS) == row_idx).astype(jnp.float32)
    col_panel = schur[0].transpose(1, 0, 2)[:, None] * first[None, :, None, None]
    corner_part = panel[0][None] * first[:, None, None, None] * top
    diag_tile = jnp.diagonal(schur, axis1=1, axis2=3)
    diag_vals = jnp.sum(jnp.where(on_diag[:, :, None], diag_tile, 0.0), axis=0)
    sizes = (col_panel.size, corner_part.size, diag_vals.size)
    packed = jnp.concatenate(
        [col_panel.reshape(-1), corner_part.reshape(-1), diag_vals.reshape(-1)]
    )
    shared = spread_sum(packed, "row", rows_n)
    col_panel = shared[: sizes[0]].reshape(nb_c, PANEL_BLOCKS, tile, tile)
    corner = shared[sizes[0] : sizes[0] + sizes[1]].reshape(width_p, width_p)
    col_diag = shared[sizes[0] + sizes[1] :].reshape(nb_c, tile)

    lower = jnp.linalg.cholesky(corner)
    logdet = 2.0 * jnp.sum(jnp.log(jnp.diagonal(lower)))
    panel_cols = col_panel.transpose(0, 3, 1, 2).reshape(nb_c * tile, width_p)
    rhs = jnp.concatenate([panel.reshape(nb_r * tile, width_p), panel_cols], axis=0)
    solved = lax.linalg.triangular_solve(
        lower, rhs, left_side=False, lower=True, transpose_a=True
    )
    factor_rows = solved[: nb_r * tile].reshape(nb_r, tile, width_p)
    factor_cols = solved[nb_r * tile :].reshape(nb_c, tile, width_p)
    update = jnp.einsum("isk,jtk->isjt", factor_rows, factor_cols, precision=highest)
    own_panel = lax.dynamic_slice_in_dim(
        factor_rows, jnp.minimum(col_idx, PANEL_BLOCKS - 1) * tile, tile, 2
    )
    in_panel = col_ids < PANEL_BLOCKS
    above = row_ids < PANEL_BLOCKS
    trailing = jnp.where(above[:, None, None, None], 0.0, schur - update)
    result = jnp.where(in_panel[None, None, :, None], own_panel[:, :, None, :], trailing)
    diag_entry = on_diag[:, None, :, None] & eye.astype(bool)[None, :, None, :]
    cleared = jnp.where(diag_entry, 0.0, result)
    factored = cleared[:, None, :, :, None, :]
    trailing_mask = (
        jnp.logical_not(above)[:, None, None, None] & jnp.logical_not(in_panel)[None, None, :, None]
    )
    rounded_update = jnp.where(trailing_mask, update, 0.0).astype(jnp.bfloat16)
    corrected = rounded_update[:, None, :, :, None, :]

    share = nblocks * tile // (rows_n * cols_n)
    start = row_idx * share
    piv_jj = start // tile
    piv_s = start % tile
    piv_block = piv_jj * cols_n + col_idx
    piv_rows = lax.dynamic_slice_in_dim(
        lax.dynamic_index_in_dim(factor_cols, piv_jj, 0, keepdims=False), piv_s, share, 0
    )
    piv_diag = lax.dynamic_slice_in_dim(
        lax.dynamic_index_in_dim(col_diag, piv_jj, 0, keepdims=False), piv_s, share, 0
    )
    trail_piv = piv_diag - jnp.sum(piv_rows * piv_rows, axis=1)
    panel_at = piv_block * tile + piv_s + jnp.arange(share)
    panel_piv = jnp.sum(
        jnp.where(panel_at[:, None] == jnp.arange(width_p)[None, :], piv_rows, 0.0), axis=1
    )
    piv = jnp.where(piv_block < PANEL_BLOCKS, panel_piv, trail_piv)
    pivots = piv.reshape(1, 1, share)
    return (factored, corrected, logdet, pivots)


def solution(mesh):
    in_specs = (P("col", "row", None), P("col", "row"), P(), P())
    out_specs = (
        P(None, "row", None, None, "col", None),
        P(None, "row", None, None, "col", None),
        P(),
        P("row", "col", None),
    )
    return jax.shard_map(body, mesh=mesh, in_specs=in_specs, out_specs=out_specs, check_vma=False)
```

```python
import jax
import jax.numpy as jnp
from jax import lax
from jax.sharding import PartitionSpec as P

PANEL_BLOCKS = 2


highest = lax.Precision.HIGHEST
user_prior = 1.0
item_prior = 1.0


def spread_sum(flat, axis, count):
    size = flat.shape[0]
    unit = count * 1024
    padded = -(-size // unit) * unit
    flat = jnp.pad(flat, (0, padded - size))
    got = lax.all_to_all(flat.reshape(count, padded // count), axis, 0, 0, tiled=True)
    part = jnp.sum(got, axis=0)
    spread = jnp.broadcast_to(part[None], (count, padded // count))
    out = lax.all_to_all(spread, axis, 0, 0, tiled=True)
    return out.reshape(padded)[:size]


def body(observed, user_effect, item_effect, block_list):
    rows_n = lax.axis_size("row")
    cols_n = lax.axis_size("col")
    row_idx = lax.axis_index("row")
    col_idx = lax.axis_index("col")
    nblocks, tile = item_effect.shape
    kcount = block_list.shape[1]
    per_row = kcount // rows_n
    slots = max(1, kcount // cols_n)
    width = kcount * tile
    group = per_row * tile
    nb_r = nblocks // rows_n
    nb_c = nblocks // cols_n
    width_p = PANEL_BLOCKS * tile
    mine = lax.dynamic_index_in_dim(block_list, col_idx, 0, keepdims=False)
    picker = (mine[:, None] == jnp.arange(nblocks)[None, :]).astype(jnp.float32)
    item_vals = jnp.dot(picker, item_effect, precision=highest).reshape(width)
    marks = observed[0]
    prob = jax.nn.sigmoid(user_effect[0][:, None] + item_vals[None, :])
    weight = jnp.where(marks > 0, prob * (1.0 - prob), 0.0)
    precision_u = user_prior + jnp.sum(weight, axis=1)
    scaled = (weight / jnp.sqrt(precision_u)[:, None]).astype(jnp.bfloat16)
    col_share = lax.psum_scatter(jnp.sum(weight, axis=0), "row", scatter_dimension=0, tiled=True)

    product = lax.dot_general(
        scaled, scaled, (((0,), (0,)), ((), ())), preferred_element_type=jnp.float32
    ).astype(jnp.bfloat16)
    grouped = product.reshape(rows_n, group, width)
    arrived = lax.all_to_all(grouped, "row", split_axis=0, concat_axis=0, tiled=True)
    cross = jnp.sum(arrived, axis=0, dtype=jnp.float32)
    global_rows = row_idx * group + jnp.arange(group)
    diag_part = jnp.where(
        global_rows[:, None] == jnp.arange(width)[None, :], col_share[:, None], 0.0
    )
    strip = (diag_part - cross).reshape(per_row, tile, kcount, tile)

    holds = mine[None, :] == jnp.arange(PANEL_BLOCKS)[:, None]
    panel_part = jnp.sum(
        jnp.where(holds[None, None, :, :, None], strip[:, :, None, :, :], 0.0), axis=3
    )
    row_ids = jnp.arange(nb_r) * rows_n + row_idx
    col_ids = jnp.arange(nb_c) * cols_n + col_idx
    eye = jnp.eye(tile, dtype=jnp.float32)
    panel_eye = jnp.where(
        (row_ids[:, None] == jnp.arange(PANEL_BLOCKS)[None, :])[:, None, :, None],
        item_prior * eye[None, :, None, :],
        0.0,
    )
    piece = tile // cols_n
    contrib = panel_part.reshape(per_row, cols_n, piece, width_p).transpose(1, 0, 2, 3)
    high = contrib.astype(jnp.bfloat16)
    low = (contrib - high.astype(jnp.float32)).astype(jnp.bfloat16)
    coded = jnp.stack([high, low], axis=1).reshape(cols_n, -1, tile)
    row_blocks_all = lax.dynamic_slice_in_dim(block_list, row_idx * per_row, per_row, 1)
    slot_of = (row_blocks_all // rows_n)[:, :, None] == jnp.arange(nb_r)[None, None, :]

    residue = block_list % cols_n
    same = residue[:, :, None] == residue[:, None, :]
    before = jnp.arange(kcount)[None, :] < jnp.arange(kcount)[:, None]
    rank = jnp.sum((same & before[None]).astype(jnp.int32), axis=2)
    my_res = lax.dynamic_index_in_dim(residue, col_idx, 0, keepdims=False)
    my_rank = lax.dynamic_index_in_dim(rank, col_idx, 0, keepdims=False)
    chooser = (
        (my_res[None, None, :] == jnp.arange(cols_n)[:, None, None])
        & (my_rank[None, None, :] == jnp.arange(slots)[None, :, None])
    ).astype(jnp.float32)
    outgoing = jnp.einsum("csk,jakb->csjab", chooser, strip, precision=highest)
    tile_rows = slots * per_row * tile
    sending = jnp.concatenate(
        [outgoing.astype(jnp.bfloat16).reshape(cols_n, tile_rows, tile), coded], axis=1
    )
    received = lax.all_to_all(sending, "col", split_axis=0, concat_axis=0, tiled=True)
    incoming = (
        received[:, :tile_rows].reshape(cols_n, slots, per_row, tile, tile).astype(jnp.float32)
    )
    coded_in = received[:, tile_rows:].reshape(cols_n, 2, per_row, piece, width_p)
    gathered = coded_in[:, 0].astype(jnp.float32) + coded_in[:, 1].astype(jnp.float32)
    part = jnp.sum(
        jnp.where(slot_of[:, :, :, None, None], gathered[:, :, None], 0.0), axis=(0, 1)
    )
    spread = jnp.broadcast_to(part[None], (cols_n, nb_r, piece, width_p))
    pieces = lax.all_to_all(spread, "col", 0, 0, tiled=True)
    panel = pieces.transpose(1, 0, 2, 3).reshape(nb_r, tile, PANEL_BLOCKS, tile) + panel_eye
    picks = (residue == col_idx)[:, None, :] & (
        rank[:, None, :] == jnp.arange(slots)[None, :, None]
    )
    col_block = jnp.sum(jnp.where(picks, block_list[:, None, :], 0), axis=2)
    valid = jnp.any(picks, axis=2)
    row_blocks = lax.dynamic_slice_in_dim(block_list, row_idx * per_row, per_row, 1)
    sel = (
        valid[:, :, None, None, None]
        & ((row_blocks[:, None, :] // rows_n)[:, :, :, None, None] == jnp.arange(nb_r)[None, None, None, :, None])
        & ((col_block[:, :, None] // cols_n)[:, :, :, None, None] == jnp.arange(nb_c)[None, None, None, None, :])
    )
    on_diag = row_ids[:, None] == col_ids[None, :]
    tiles = jnp.einsum(
        "cvjiq,cvjst->isqt",
        sel.astype(jnp.float32),
        incoming,
        precision=highest,
    )
    schur = tiles + jnp.where(on_diag[:, None, :, None], item_prior * eye[None, :, None, :], 0.0)

    top = (row_idx < PANEL_BLOCKS).astype(jnp.float32)
    first = (jnp.arange(PANEL_BLOCKS) == row_idx).astype(jnp.float32)
    col_panel = schur[0].transpose(1, 0, 2)[:, None] * first[None, :, None, None]
    corner_part = panel[0][None] * first[:, None, None, None] * top
    diag_tile = jnp.diagonal(schur, axis1=1, axis2=3)
    diag_vals = jnp.sum(jnp.where(on_diag[:, :, None], diag_tile, 0.0), axis=0)
    corner = spread_sum(corner_part.reshape(-1), "row", rows_n).reshape(width_p, width_p)
    lower = jnp.linalg.cholesky(corner)
    logdet = 2.0 * jnp.sum(jnp.log(jnp.diagonal(lower)))
    inv_lower = lax.linalg.triangular_solve(
        lower, jnp.eye(width_p, dtype=jnp.float32), left_side=True, lower=True
    )
    factor_rows = jnp.einsum(
        "isk,mk->ism", panel.reshape(nb_r, tile, width_p), inv_lower, precision=highest
    )
    sizes = (col_panel.size, diag_vals.size)
    packed = jnp.concatenate([col_panel.reshape(-1), diag_vals.reshape(-1)])
    shared = spread_sum(packed, "row", rows_n)
    col_panel = shared[: sizes[0]].reshape(nb_c, PANEL_BLOCKS, tile, tile)
    col_diag = shared[sizes[0] :].reshape(nb_c, tile)
    panel_cols = col_panel.transpose(0, 3, 1, 2).reshape(nb_c, tile, width_p)
    factor_cols = jnp.einsum("jtk,mk->jtm", panel_cols, inv_lower, precision=highest)
    update = jnp.einsum("isk,jtk->isjt", factor_rows, factor_cols, precision=highest)
    own_panel = lax.dynamic_slice_in_dim(
        factor_rows, jnp.minimum(col_idx, PANEL_BLOCKS - 1) * tile, tile, 2
    )
    in_panel = col_ids < PANEL_BLOCKS
    above = row_ids < PANEL_BLOCKS
    trailing = jnp.where(above[:, None, None, None], 0.0, schur - update)
    result = jnp.where(in_panel[None, None, :, None], own_panel[:, :, None, :], trailing)
    diag_entry = on_diag[:, None, :, None] & eye.astype(bool)[None, :, None, :]
    cleared = jnp.where(diag_entry, 0.0, result)
    factored = cleared[:, None, :, :, None, :]
    trailing_mask = (
        jnp.logical_not(above)[:, None, None, None] & jnp.logical_not(in_panel)[None, None, :, None]
    )
    rounded_update = jnp.where(trailing_mask, update, 0.0).astype(jnp.bfloat16)
    corrected = rounded_update[:, None, :, :, None, :]

    share = nblocks * tile // (rows_n * cols_n)
    start = row_idx * share
    piv_jj = start // tile
    piv_s = start % tile
    piv_block = piv_jj * cols_n + col_idx
    piv_rows = lax.dynamic_slice_in_dim(
        lax.dynamic_index_in_dim(factor_cols, piv_jj, 0, keepdims=False), piv_s, share, 0
    )
    piv_diag = lax.dynamic_slice_in_dim(
        lax.dynamic_index_in_dim(col_diag, piv_jj, 0, keepdims=False), piv_s, share, 0
    )
    trail_piv = piv_diag - jnp.sum(piv_rows * piv_rows, axis=1)
    panel_at = piv_block * tile + piv_s + jnp.arange(share)
    panel_piv = jnp.sum(
        jnp.where(panel_at[:, None] == jnp.arange(width_p)[None, :], piv_rows, 0.0), axis=1
    )
    piv = jnp.where(piv_block < PANEL_BLOCKS, panel_piv, trail_piv)
    pivots = piv.reshape(1, 1, share)
    return (factored, corrected, logdet, pivots)


def solution(mesh):
    in_specs = (P("col", "row", None), P("col", "row"), P(), P())
    out_specs = (
        P(None, "row", None, None, "col", None),
        P(None, "row", None, None, "col", None),
        P(),
        P("row", "col", None),
    )
    return jax.shard_map(body, mesh=mesh, in_specs=in_specs, out_specs=out_specs, check_vma=False)
```

```python
import jax
import jax.numpy as jnp
from jax import lax
from jax.sharding import PartitionSpec as P

PANEL_BLOCKS = 2


highest = lax.Precision.HIGHEST
user_prior = 1.0
item_prior = 1.0


def spread_sum(flat, axis, count):
    size = flat.shape[0]
    unit = count * 1024
    padded = -(-size // unit) * unit
    flat = jnp.pad(flat, (0, padded - size))
    got = lax.all_to_all(flat.reshape(count, padded // count), axis, 0, 0, tiled=True)
    part = jnp.sum(got, axis=0)
    spread = jnp.broadcast_to(part[None], (count, padded // count))
    out = lax.all_to_all(spread, axis, 0, 0, tiled=True)
    return out.reshape(padded)[:size]


def body(observed, user_effect, item_effect, block_list):
    rows_n = lax.axis_size("row")
    cols_n = lax.axis_size("col")
    row_idx = lax.axis_index("row")
    col_idx = lax.axis_index("col")
    nblocks, tile = item_effect.shape
    kcount = block_list.shape[1]
    per_row = kcount // rows_n
    slots = max(1, kcount // cols_n)
    width = kcount * tile
    group = per_row * tile
    nb_r = nblocks // rows_n
    nb_c = nblocks // cols_n
    width_p = PANEL_BLOCKS * tile
    mine = lax.dynamic_index_in_dim(block_list, col_idx, 0, keepdims=False)
    picker = (mine[:, None] == jnp.arange(nblocks)[None, :]).astype(jnp.float32)
    item_vals = jnp.dot(picker, item_effect, precision=highest).reshape(width)
    marks = observed[0]
    prob = jax.nn.sigmoid(user_effect[0][:, None] + item_vals[None, :])
    weight = jnp.where(marks > 0, prob * (1.0 - prob), 0.0)
    precision_u = user_prior + jnp.sum(weight, axis=1)
    scaled = (weight / jnp.sqrt(precision_u)[:, None]).astype(jnp.bfloat16)
    col_share = lax.psum_scatter(jnp.sum(weight, axis=0), "row", scatter_dimension=0, tiled=True)

    product = lax.dot_general(
        scaled, scaled, (((0,), (0,)), ((), ())), preferred_element_type=jnp.float32
    ).astype(jnp.bfloat16)
    grouped = product.reshape(rows_n, group, width)
    arrived = lax.all_to_all(grouped, "row", split_axis=0, concat_axis=0, tiled=True)
    cross = jnp.sum(arrived, axis=0, dtype=jnp.float32)
    global_rows = row_idx * group + jnp.arange(group)
    diag_part = jnp.where(
        global_rows[:, None] == jnp.arange(width)[None, :], col_share[:, None], 0.0
    )
    strip = (diag_part - cross).reshape(per_row, tile, kcount, tile)

    holds = mine[None, :] == jnp.arange(PANEL_BLOCKS)[:, None]
    panel_part = jnp.sum(
        jnp.where(holds[None, None, :, :, None], strip[:, :, None, :, :], 0.0), axis=3
    )
    row_ids = jnp.arange(nb_r) * rows_n + row_idx
    col_ids = jnp.arange(nb_c) * cols_n + col_idx
    eye = jnp.eye(tile, dtype=jnp.float32)
    panel_eye = jnp.where(
        (row_ids[:, None] == jnp.arange(PANEL_BLOCKS)[None, :])[:, None, :, None],
        item_prior * eye[None, :, None, :],
        0.0,
    )
    piece = tile // cols_n
    contrib = panel_part.reshape(per_row, cols_n, piece, width_p).transpose(1, 0, 2, 3)
    scaled_up = contrib * 65537.0
    head = scaled_up - (scaled_up - contrib)
    high = head.astype(jnp.bfloat16)
    low = (contrib - head).astype(jnp.bfloat16)
    coded = jnp.stack([high, low], axis=1).reshape(cols_n, -1, tile)
    row_blocks_all = lax.dynamic_slice_in_dim(block_list, row_idx * per_row, per_row, 1)
    slot_of = (row_blocks_all // rows_n)[:, :, None] == jnp.arange(nb_r)[None, None, :]

    residue = block_list % cols_n
    same = residue[:, :, None] == residue[:, None, :]
    before = jnp.arange(kcount)[None, :] < jnp.arange(kcount)[:, None]
    rank = jnp.sum((same & before[None]).astype(jnp.int32), axis=2)
    my_res = lax.dynamic_index_in_dim(residue, col_idx, 0, keepdims=False)
    my_rank = lax.dynamic_index_in_dim(rank, col_idx, 0, keepdims=False)
    chooser = (
        (my_res[None, None, :] == jnp.arange(cols_n)[:, None, None])
        & (my_rank[None, None, :] == jnp.arange(slots)[None, :, None])
    ).astype(jnp.float32)
    outgoing = jnp.einsum("csk,jakb->csjab", chooser, strip, precision=highest)
    tile_rows = slots * per_row * tile
    sending = jnp.concatenate(
        [outgoing.astype(jnp.bfloat16).reshape(cols_n, tile_rows, tile), coded], axis=1
    )
    received = lax.all_to_all(sending, "col", split_axis=0, concat_axis=0, tiled=True)
    incoming = (
        received[:, :tile_rows].reshape(cols_n, slots, per_row, tile, tile).astype(jnp.float32)
    )
    coded_in = received[:, tile_rows:].reshape(cols_n, 2, per_row, piece, width_p)
    gathered = coded_in[:, 0].astype(jnp.float32) + coded_in[:, 1].astype(jnp.float32)
    part = jnp.sum(
        jnp.where(slot_of[:, :, :, None, None], gathered[:, :, None], 0.0), axis=(0, 1)
    )
    first = (jnp.arange(PANEL_BLOCKS) == row_idx).astype(jnp.float32)
    corner_piece = part[0][None] * first[:, None, None]
    corner_piece = spread_sum(corner_piece.reshape(-1), "row", rows_n)
    corner_spread = jnp.broadcast_to(
        corner_piece.reshape(1, PANEL_BLOCKS, piece, width_p), (cols_n, PANEL_BLOCKS, piece, width_p)
    )
    corner_all = lax.all_to_all(corner_spread, "col", 0, 0, tiled=True)
    corner = corner_all.transpose(1, 0, 2, 3).reshape(width_p, width_p) + item_prior * jnp.eye(
        width_p, dtype=jnp.float32
    )
    spread = jnp.broadcast_to(part[None], (cols_n, nb_r, piece, width_p))
    pieces = lax.all_to_all(spread, "col", 0, 0, tiled=True)
    panel = pieces.transpose(1, 0, 2, 3).reshape(nb_r, tile, PANEL_BLOCKS, tile) + panel_eye
    picks = (residue == col_idx)[:, None, :] & (
        rank[:, None, :] == jnp.arange(slots)[None, :, None]
    )
    col_block = jnp.sum(jnp.where(picks, block_list[:, None, :], 0), axis=2)
    valid = jnp.any(picks, axis=2)
    row_blocks = lax.dynamic_slice_in_dim(block_list, row_idx * per_row, per_row, 1)
    sel = (
        valid[:, :, None, None, None]
        & ((row_blocks[:, None, :] // rows_n)[:, :, :, None, None] == jnp.arange(nb_r)[None, None, None, :, None])
        & ((col_block[:, :, None] // cols_n)[:, :, :, None, None] == jnp.arange(nb_c)[None, None, None, None, :])
    )
    on_diag = row_ids[:, None] == col_ids[None, :]
    tiles = jnp.einsum(
        "cvjiq,cvjst->isqt",
        sel.astype(jnp.float32),
        incoming,
        precision=highest,
    )
    schur = tiles + jnp.where(on_diag[:, None, :, None], item_prior * eye[None, :, None, :], 0.0)

    col_panel = schur[0].transpose(1, 0, 2)[:, None] * first[None, :, None, None]
    diag_tile = jnp.diagonal(schur, axis1=1, axis2=3)
    diag_vals = jnp.sum(jnp.where(on_diag[:, :, None], diag_tile, 0.0), axis=0)
    lower = jnp.linalg.cholesky(corner)
    logdet = 2.0 * jnp.sum(jnp.log(jnp.diagonal(lower)))
    inv_lower = lax.linalg.triangular_solve(
        lower, jnp.eye(width_p, dtype=jnp.float32), left_side=True, lower=True
    )
    factor_rows = jnp.einsum(
        "isk,mk->ism", panel.reshape(nb_r, tile, width_p), inv_lower, precision=highest
    )
    sizes = (col_panel.size, diag_vals.size)
    packed = jnp.concatenate([col_panel.reshape(-1), diag_vals.reshape(-1)])
    shared = spread_sum(packed, "row", rows_n)
    col_panel = shared[: sizes[0]].reshape(nb_c, PANEL_BLOCKS, tile, tile)
    col_diag = shared[sizes[0] :].reshape(nb_c, tile)
    panel_cols = col_panel.transpose(0, 3, 1, 2).reshape(nb_c, tile, width_p)
    factor_cols = jnp.einsum("jtk,mk->jtm", panel_cols, inv_lower, precision=highest)
    update = jnp.einsum("isk,jtk->isjt", factor_rows, factor_cols, precision=highest)
    own_panel = lax.dynamic_slice_in_dim(
        factor_rows, jnp.minimum(col_idx, PANEL_BLOCKS - 1) * tile, tile, 2
    )
    in_panel = col_ids < PANEL_BLOCKS
    above = row_ids < PANEL_BLOCKS
    trailing = jnp.where(above[:, None, None, None], 0.0, schur - update)
    result = jnp.where(in_panel[None, None, :, None], own_panel[:, :, None, :], trailing)
    diag_entry = on_diag[:, None, :, None] & eye.astype(bool)[None, :, None, :]
    cleared = jnp.where(diag_entry, 0.0, result)
    factored = cleared[:, None, :, :, None, :]
    trailing_mask = (
        jnp.logical_not(above)[:, None, None, None] & jnp.logical_not(in_panel)[None, None, :, None]
    )
    rounded_update = jnp.where(trailing_mask, update, 0.0).astype(jnp.bfloat16)
    corrected = rounded_update[:, None, :, :, None, :]

    share = nblocks * tile // (rows_n * cols_n)
    start = row_idx * share
    piv_jj = start // tile
    piv_s = start % tile
    piv_block = piv_jj * cols_n + col_idx
    piv_rows = lax.dynamic_slice_in_dim(
        lax.dynamic_index_in_dim(factor_cols, piv_jj, 0, keepdims=False), piv_s, share, 0
    )
    piv_diag = lax.dynamic_slice_in_dim(
        lax.dynamic_index_in_dim(col_diag, piv_jj, 0, keepdims=False), piv_s, share, 0
    )
    trail_piv = piv_diag - jnp.sum(piv_rows * piv_rows, axis=1)
    panel_at = piv_block * tile + piv_s + jnp.arange(share)
    panel_piv = jnp.sum(
        jnp.where(panel_at[:, None] == jnp.arange(width_p)[None, :], piv_rows, 0.0), axis=1
    )
    piv = jnp.where(piv_block < PANEL_BLOCKS, panel_piv, trail_piv)
    pivots = piv.reshape(1, 1, share)
    return (factored, corrected, logdet, pivots)


def solution(mesh):
    in_specs = (P("col", "row", None), P("col", "row"), P(), P())
    out_specs = (
        P(None, "row", None, None, "col", None),
        P(None, "row", None, None, "col", None),
        P(),
        P("row", "col", None),
    )
    return jax.shard_map(body, mesh=mesh, in_specs=in_specs, out_specs=out_specs, check_vma=False)
```

```python
import jax
import jax.numpy as jnp
from jax import lax
from jax.sharding import PartitionSpec as P

PANEL_BLOCKS = 2


highest = lax.Precision.HIGHEST
user_prior = 1.0
item_prior = 1.0


def spread_sum(flat, axis, count):
    size = flat.shape[0]
    unit = count * 1024
    padded = -(-size // unit) * unit
    flat = jnp.pad(flat, (0, padded - size))
    got = lax.all_to_all(flat.reshape(count, padded // count), axis, 0, 0, tiled=True)
    part = jnp.sum(got, axis=0)
    spread = jnp.broadcast_to(part[None], (count, padded // count))
    out = lax.all_to_all(spread, axis, 0, 0, tiled=True)
    return out.reshape(padded)[:size]


def body(observed, user_effect, item_effect, block_list):
    rows_n = lax.axis_size("row")
    cols_n = lax.axis_size("col")
    row_idx = lax.axis_index("row")
    col_idx = lax.axis_index("col")
    nblocks, tile = item_effect.shape
    kcount = block_list.shape[1]
    per_row = kcount // rows_n
    slots = max(1, kcount // cols_n)
    width = kcount * tile
    group = per_row * tile
    nb_r = nblocks // rows_n
    nb_c = nblocks // cols_n
    width_p = PANEL_BLOCKS * tile
    mine = lax.dynamic_index_in_dim(block_list, col_idx, 0, keepdims=False)
    picker = (mine[:, None] == jnp.arange(nblocks)[None, :]).astype(jnp.float32)
    item_vals = jnp.dot(picker, item_effect, precision=highest).reshape(width)
    marks = observed[0]
    prob = jax.nn.sigmoid(user_effect[0][:, None] + item_vals[None, :])
    weight = jnp.where(marks > 0, prob * (1.0 - prob), 0.0)
    precision_u = user_prior + jnp.sum(weight, axis=1)
    scaled = (weight / jnp.sqrt(precision_u)[:, None]).astype(jnp.bfloat16)
    col_share = lax.psum_scatter(jnp.sum(weight, axis=0), "row", scatter_dimension=0, tiled=True)

    product = lax.dot_general(
        scaled, scaled, (((0,), (0,)), ((), ())), preferred_element_type=jnp.float32
    ).astype(jnp.bfloat16)
    grouped = product.reshape(rows_n, group, width)
    arrived = lax.all_to_all(grouped, "row", split_axis=0, concat_axis=0, tiled=True)
    cross = jnp.sum(arrived, axis=0, dtype=jnp.float32)
    global_rows = row_idx * group + jnp.arange(group)
    diag_part = jnp.where(
        global_rows[:, None] == jnp.arange(width)[None, :], col_share[:, None], 0.0
    )
    strip = (diag_part - cross).reshape(per_row, tile, kcount, tile)

    holds = mine[None, :] == jnp.arange(PANEL_BLOCKS)[:, None]
    panel_part = jnp.sum(
        jnp.where(holds[None, None, :, :, None], strip[:, :, None, :, :], 0.0), axis=3
    )
    row_ids = jnp.arange(nb_r) * rows_n + row_idx
    col_ids = jnp.arange(nb_c) * cols_n + col_idx
    eye = jnp.eye(tile, dtype=jnp.float32)
    panel_eye = jnp.where(
        (row_ids[:, None] == jnp.arange(PANEL_BLOCKS)[None, :])[:, None, :, None],
        item_prior * eye[None, :, None, :],
        0.0,
    )
    piece = tile // cols_n
    contrib = panel_part.reshape(per_row, cols_n, piece, width_p).transpose(1, 0, 2, 3)
    scaled_up = contrib * 65537.0
    head = scaled_up - (scaled_up - contrib)
    high = head.astype(jnp.bfloat16)
    low = (contrib - head).astype(jnp.bfloat16)
    coded = jnp.stack([high, low], axis=1).reshape(cols_n, -1, tile)
    row_blocks_all = lax.dynamic_slice_in_dim(block_list, row_idx * per_row, per_row, 1)
    slot_of = (row_blocks_all // rows_n)[:, :, None] == jnp.arange(nb_r)[None, None, :]

    residue = block_list % cols_n
    same = residue[:, :, None] == residue[:, None, :]
    before = jnp.arange(kcount)[None, :] < jnp.arange(kcount)[:, None]
    rank = jnp.sum((same & before[None]).astype(jnp.int32), axis=2)
    my_res = lax.dynamic_index_in_dim(residue, col_idx, 0, keepdims=False)
    my_rank = lax.dynamic_index_in_dim(rank, col_idx, 0, keepdims=False)
    chooser = (
        (my_res[None, None, :] == jnp.arange(cols_n)[:, None, None])
        & (my_rank[None, None, :] == jnp.arange(slots)[None, :, None])
    ).astype(jnp.float32)
    outgoing = jnp.einsum("csk,jakb->csjab", chooser, strip, precision=highest)
    tile_rows = slots * per_row * tile
    sending = jnp.concatenate(
        [outgoing.astype(jnp.bfloat16).reshape(cols_n, tile_rows, tile), coded], axis=1
    )
    received = lax.all_to_all(sending, "col", split_axis=0, concat_axis=0, tiled=True)
    incoming = (
        received[:, :tile_rows].reshape(cols_n, slots, per_row, tile, tile).astype(jnp.float32)
    )
    coded_in = received[:, tile_rows:].reshape(cols_n, 2, per_row, piece, width_p)
    gathered = coded_in[:, 0].astype(jnp.float32) + coded_in[:, 1].astype(jnp.float32)
    part = jnp.sum(
        jnp.where(slot_of[:, :, :, None, None], gathered[:, :, None], 0.0), axis=(0, 1)
    )
    first = (jnp.arange(PANEL_BLOCKS) == row_idx).astype(jnp.float32)
    corner_piece = part[0][None] * first[:, None, None]
    corner_piece = spread_sum(corner_piece.reshape(-1), "row", rows_n)
    corner_spread = jnp.broadcast_to(
        corner_piece.reshape(1, PANEL_BLOCKS, piece, width_p), (cols_n, PANEL_BLOCKS, piece, width_p)
    )
    corner_all = lax.all_to_all(corner_spread, "col", 0, 0, tiled=True)
    corner = corner_all.transpose(1, 0, 2, 3).reshape(width_p, width_p) + item_prior * jnp.eye(
        width_p, dtype=jnp.float32
    )
    spread = jnp.broadcast_to(part[None], (cols_n, nb_r, piece, width_p))
    spread, corner = lax.optimization_barrier((spread, corner))
    pieces = lax.all_to_all(spread, "col", 0, 0, tiled=True)
    panel = pieces.transpose(1, 0, 2, 3).reshape(nb_r, tile, PANEL_BLOCKS, tile) + panel_eye
    picks = (residue == col_idx)[:, None, :] & (
        rank[:, None, :] == jnp.arange(slots)[None, :, None]
    )
    col_block = jnp.sum(jnp.where(picks, block_list[:, None, :], 0), axis=2)
    valid = jnp.any(picks, axis=2)
    row_blocks = lax.dynamic_slice_in_dim(block_list, row_idx * per_row, per_row, 1)
    sel = (
        valid[:, :, None, None, None]
        & ((row_blocks[:, None, :] // rows_n)[:, :, :, None, None] == jnp.arange(nb_r)[None, None, None, :, None])
        & ((col_block[:, :, None] // cols_n)[:, :, :, None, None] == jnp.arange(nb_c)[None, None, None, None, :])
    )
    on_diag = row_ids[:, None] == col_ids[None, :]
    tiles = jnp.einsum(
        "cvjiq,cvjst->isqt",
        sel.astype(jnp.float32),
        incoming,
        precision=highest,
    )
    schur = tiles + jnp.where(on_diag[:, None, :, None], item_prior * eye[None, :, None, :], 0.0)

    col_panel = schur[0].transpose(1, 0, 2)[:, None] * first[None, :, None, None]
    diag_tile = jnp.diagonal(schur, axis1=1, axis2=3)
    diag_vals = jnp.sum(jnp.where(on_diag[:, :, None], diag_tile, 0.0), axis=0)
    lower = jnp.linalg.cholesky(corner)
    logdet = 2.0 * jnp.sum(jnp.log(jnp.diagonal(lower)))
    inv_lower = lax.linalg.triangular_solve(
        lower, jnp.eye(width_p, dtype=jnp.float32), left_side=True, lower=True
    )
    factor_rows = jnp.einsum(
        "isk,mk->ism", panel.reshape(nb_r, tile, width_p), inv_lower, precision=highest
    )
    sizes = (col_panel.size, diag_vals.size)
    packed = jnp.concatenate([col_panel.reshape(-1), diag_vals.reshape(-1)])
    packed, lower = lax.optimization_barrier((packed, lower))
    shared = spread_sum(packed, "row", rows_n)
    col_panel = shared[: sizes[0]].reshape(nb_c, PANEL_BLOCKS, tile, tile)
    col_diag = shared[sizes[0] :].reshape(nb_c, tile)
    panel_cols = col_panel.transpose(0, 3, 1, 2).reshape(nb_c, tile, width_p)
    factor_cols = jnp.einsum("jtk,mk->jtm", panel_cols, inv_lower, precision=highest)
    update = jnp.einsum("isk,jtk->isjt", factor_rows, factor_cols, precision=highest)
    own_panel = lax.dynamic_slice_in_dim(
        factor_rows, jnp.minimum(col_idx, PANEL_BLOCKS - 1) * tile, tile, 2
    )
    in_panel = col_ids < PANEL_BLOCKS
    above = row_ids < PANEL_BLOCKS
    trailing = jnp.where(above[:, None, None, None], 0.0, schur - update)
    result = jnp.where(in_panel[None, None, :, None], own_panel[:, :, None, :], trailing)
    diag_entry = on_diag[:, None, :, None] & eye.astype(bool)[None, :, None, :]
    cleared = jnp.where(diag_entry, 0.0, result)
    factored = cleared[:, None, :, :, None, :]
    trailing_mask = (
        jnp.logical_not(above)[:, None, None, None] & jnp.logical_not(in_panel)[None, None, :, None]
    )
    rounded_update = jnp.where(trailing_mask, update, 0.0).astype(jnp.bfloat16)
    corrected = rounded_update[:, None, :, :, None, :]

    share = nblocks * tile // (rows_n * cols_n)
    start = row_idx * share
    piv_jj = start // tile
    piv_s = start % tile
    piv_block = piv_jj * cols_n + col_idx
    piv_rows = lax.dynamic_slice_in_dim(
        lax.dynamic_index_in_dim(factor_cols, piv_jj, 0, keepdims=False), piv_s, share, 0
    )
    piv_diag = lax.dynamic_slice_in_dim(
        lax.dynamic_index_in_dim(col_diag, piv_jj, 0, keepdims=False), piv_s, share, 0
    )
    trail_piv = piv_diag - jnp.sum(piv_rows * piv_rows, axis=1)
    panel_at = piv_block * tile + piv_s + jnp.arange(share)
    panel_piv = jnp.sum(
        jnp.where(panel_at[:, None] == jnp.arange(width_p)[None, :], piv_rows, 0.0), axis=1
    )
    piv = jnp.where(piv_block < PANEL_BLOCKS, panel_piv, trail_piv)
    pivots = piv.reshape(1, 1, share)
    return (factored, corrected, logdet, pivots)


def solution(mesh):
    in_specs = (P("col", "row", None), P("col", "row"), P(), P())
    out_specs = (
        P(None, "row", None, None, "col", None),
        P(None, "row", None, None, "col", None),
        P(),
        P("row", "col", None),
    )
    return jax.shard_map(body, mesh=mesh, in_specs=in_specs, out_specs=out_specs, check_vma=False)
```

```python
import jax
import jax.numpy as jnp
from jax import lax
from jax.sharding import PartitionSpec as P

PANEL_BLOCKS = 2


highest = lax.Precision.HIGHEST
user_prior = 1.0
item_prior = 1.0


def spread_sum(flat, axis, count):
    size = flat.shape[0]
    unit = count * 1024
    padded = -(-size // unit) * unit
    flat = jnp.pad(flat, (0, padded - size))
    lanes = padded // count // 128
    got = lax.all_to_all(flat.reshape(count, lanes, 128), axis, 0, 0, tiled=True)
    part = jnp.sum(got, axis=0)
    spread = jnp.broadcast_to(part[None], (count, lanes, 128))
    out = lax.all_to_all(spread, axis, 0, 0, tiled=True)
    return out.reshape(padded)[:size]


def body(observed, user_effect, item_effect, block_list):
    rows_n = lax.axis_size("row")
    cols_n = lax.axis_size("col")
    row_idx = lax.axis_index("row")
    col_idx = lax.axis_index("col")
    nblocks, tile = item_effect.shape
    kcount = block_list.shape[1]
    per_row = kcount // rows_n
    slots = max(1, kcount // cols_n)
    width = kcount * tile
    group = per_row * tile
    nb_r = nblocks // rows_n
    nb_c = nblocks // cols_n
    width_p = PANEL_BLOCKS * tile
    mine = lax.dynamic_index_in_dim(block_list, col_idx, 0, keepdims=False)
    picker = (mine[:, None] == jnp.arange(nblocks)[None, :]).astype(jnp.float32)
    item_vals = jnp.dot(picker, item_effect, precision=highest).reshape(width)
    marks = observed[0]
    prob = jax.nn.sigmoid(user_effect[0][:, None] + item_vals[None, :])
    weight = jnp.where(marks > 0, prob * (1.0 - prob), 0.0)
    precision_u = user_prior + jnp.sum(weight, axis=1)
    scaled = (weight / jnp.sqrt(precision_u)[:, None]).astype(jnp.bfloat16)
    col_share = lax.psum_scatter(jnp.sum(weight, axis=0), "row", scatter_dimension=0, tiled=True)

    product = lax.dot_general(
        scaled, scaled, (((0,), (0,)), ((), ())), preferred_element_type=jnp.float32
    ).astype(jnp.bfloat16)
    grouped = product.reshape(rows_n, group, width)
    arrived = lax.all_to_all(grouped, "row", split_axis=0, concat_axis=0, tiled=True)
    cross = jnp.sum(arrived, axis=0, dtype=jnp.float32)
    global_rows = row_idx * group + jnp.arange(group)
    diag_part = jnp.where(
        global_rows[:, None] == jnp.arange(width)[None, :], col_share[:, None], 0.0
    )
    strip = (diag_part - cross).reshape(per_row, tile, kcount, tile)

    holds = mine[None, :] == jnp.arange(PANEL_BLOCKS)[:, None]
    panel_part = jnp.sum(
        jnp.where(holds[None, None, :, :, None], strip[:, :, None, :, :], 0.0), axis=3
    )
    row_ids = jnp.arange(nb_r) * rows_n + row_idx
    col_ids = jnp.arange(nb_c) * cols_n + col_idx
    eye = jnp.eye(tile, dtype=jnp.float32)
    panel_eye = jnp.where(
        (row_ids[:, None] == jnp.arange(PANEL_BLOCKS)[None, :])[:, None, :, None],
        item_prior * eye[None, :, None, :],
        0.0,
    )
    piece = tile // cols_n
    contrib = panel_part.reshape(per_row, cols_n, piece, width_p).transpose(1, 0, 2, 3)
    scaled_up = contrib * 65537.0
    head = scaled_up - (scaled_up - contrib)
    high = head.astype(jnp.bfloat16)
    low = (contrib - head).astype(jnp.bfloat16)
    coded = jnp.stack([high, low], axis=1).reshape(cols_n, -1, tile)
    row_blocks_all = lax.dynamic_slice_in_dim(block_list, row_idx * per_row, per_row, 1)
    slot_of = (row_blocks_all // rows_n)[:, :, None] == jnp.arange(nb_r)[None, None, :]

    residue = block_list % cols_n
    same = residue[:, :, None] == residue[:, None, :]
    before = jnp.arange(kcount)[None, :] < jnp.arange(kcount)[:, None]
    rank = jnp.sum((same & before[None]).astype(jnp.int32), axis=2)
    my_res = lax.dynamic_index_in_dim(residue, col_idx, 0, keepdims=False)
    my_rank = lax.dynamic_index_in_dim(rank, col_idx, 0, keepdims=False)
    chooser = (
        (my_res[None, None, :] == jnp.arange(cols_n)[:, None, None])
        & (my_rank[None, None, :] == jnp.arange(slots)[None, :, None])
    ).astype(jnp.float32)
    outgoing = jnp.einsum("csk,jakb->csjab", chooser, strip, precision=highest)
    tile_rows = slots * per_row * tile
    sending = jnp.concatenate(
        [outgoing.astype(jnp.bfloat16).reshape(cols_n, tile_rows, tile), coded], axis=1
    )
    received = lax.all_to_all(sending, "col", split_axis=0, concat_axis=0, tiled=True)
    incoming = (
        received[:, :tile_rows].reshape(cols_n, slots, per_row, tile, tile).astype(jnp.float32)
    )
    coded_in = received[:, tile_rows:].reshape(cols_n, 2, per_row, piece, width_p)
    gathered = coded_in[:, 0].astype(jnp.float32) + coded_in[:, 1].astype(jnp.float32)
    part = jnp.sum(
        jnp.where(slot_of[:, :, :, None, None], gathered[:, :, None], 0.0), axis=(0, 1)
    )
    first = (jnp.arange(PANEL_BLOCKS) == row_idx).astype(jnp.float32)
    corner_piece = part[0][None] * first[:, None, None]
    corner_piece = spread_sum(corner_piece.reshape(-1), "row", rows_n)
    corner_spread = jnp.broadcast_to(
        corner_piece.reshape(1, PANEL_BLOCKS, piece, width_p), (cols_n, PANEL_BLOCKS, piece, width_p)
    )
    corner_all = lax.all_to_all(corner_spread, "col", 0, 0, tiled=True)
    corner = corner_all.transpose(1, 0, 2, 3).reshape(width_p, width_p) + item_prior * jnp.eye(
        width_p, dtype=jnp.float32
    )
    spread = jnp.broadcast_to(part[None], (cols_n, nb_r, piece, width_p))
    pieces = lax.all_to_all(spread, "col", 0, 0, tiled=True)
    panel = pieces.transpose(1, 0, 2, 3).reshape(nb_r, tile, PANEL_BLOCKS, tile) + panel_eye
    picks = (residue == col_idx)[:, None, :] & (
        rank[:, None, :] == jnp.arange(slots)[None, :, None]
    )
    col_block = jnp.sum(jnp.where(picks, block_list[:, None, :], 0), axis=2)
    valid = jnp.any(picks, axis=2)
    row_blocks = lax.dynamic_slice_in_dim(block_list, row_idx * per_row, per_row, 1)
    sel = (
        valid[:, :, None, None, None]
        & ((row_blocks[:, None, :] // rows_n)[:, :, :, None, None] == jnp.arange(nb_r)[None, None, None, :, None])
        & ((col_block[:, :, None] // cols_n)[:, :, :, None, None] == jnp.arange(nb_c)[None, None, None, None, :])
    )
    on_diag = row_ids[:, None] == col_ids[None, :]
    tiles = jnp.einsum(
        "cvjiq,cvjst->isqt",
        sel.astype(jnp.float32),
        incoming,
        precision=highest,
    )
    schur = tiles + jnp.where(on_diag[:, None, :, None], item_prior * eye[None, :, None, :], 0.0)

    col_panel = schur[0].transpose(1, 0, 2)[:, None] * first[None, :, None, None]
    diag_tile = jnp.diagonal(schur, axis1=1, axis2=3)
    diag_vals = jnp.sum(jnp.where(on_diag[:, :, None], diag_tile, 0.0), axis=0)
    lower = jnp.linalg.cholesky(corner)
    logdet = 2.0 * jnp.sum(jnp.log(jnp.diagonal(lower)))
    inv_lower = lax.linalg.triangular_solve(
        lower, jnp.eye(width_p, dtype=jnp.float32), left_side=True, lower=True
    )
    factor_rows = jnp.einsum(
        "isk,mk->ism", panel.reshape(nb_r, tile, width_p), inv_lower, precision=highest
    )
    sizes = (col_panel.size, diag_vals.size)
    packed = jnp.concatenate([col_panel.reshape(-1), diag_vals.reshape(-1)])
    shared = spread_sum(packed, "row", rows_n)
    col_panel = shared[: sizes[0]].reshape(nb_c, PANEL_BLOCKS, tile, tile)
    col_diag = shared[sizes[0] :].reshape(nb_c, tile)
    panel_cols = col_panel.transpose(0, 3, 1, 2).reshape(nb_c, tile, width_p)
    factor_cols = jnp.einsum("jtk,mk->jtm", panel_cols, inv_lower, precision=highest)
    update = jnp.einsum("isk,jtk->isjt", factor_rows, factor_cols, precision=highest)
    own_panel = lax.dynamic_slice_in_dim(
        factor_rows, jnp.minimum(col_idx, PANEL_BLOCKS - 1) * tile, tile, 2
    )
    in_panel = col_ids < PANEL_BLOCKS
    above = row_ids < PANEL_BLOCKS
    trailing = jnp.where(above[:, None, None, None], 0.0, schur - update)
    result = jnp.where(in_panel[None, None, :, None], own_panel[:, :, None, :], trailing)
    diag_entry = on_diag[:, None, :, None] & eye.astype(bool)[None, :, None, :]
    cleared = jnp.where(diag_entry, 0.0, result)
    factored = cleared[:, None, :, :, None, :]
    trailing_mask = (
        jnp.logical_not(above)[:, None, None, None] & jnp.logical_not(in_panel)[None, None, :, None]
    )
    rounded_update = jnp.where(trailing_mask, update, 0.0).astype(jnp.bfloat16)
    corrected = rounded_update[:, None, :, :, None, :]

    share = nblocks * tile // (rows_n * cols_n)
    start = row_idx * share
    piv_jj = start // tile
    piv_s = start % tile
    piv_block = piv_jj * cols_n + col_idx
    piv_rows = lax.dynamic_slice_in_dim(
        lax.dynamic_index_in_dim(factor_cols, piv_jj, 0, keepdims=False), piv_s, share, 0
    )
    piv_diag = lax.dynamic_slice_in_dim(
        lax.dynamic_index_in_dim(col_diag, piv_jj, 0, keepdims=False), piv_s, share, 0
    )
    trail_piv = piv_diag - jnp.sum(piv_rows * piv_rows, axis=1)
    panel_at = piv_block * tile + piv_s + jnp.arange(share)
    panel_piv = jnp.sum(
        jnp.where(panel_at[:, None] == jnp.arange(width_p)[None, :], piv_rows, 0.0), axis=1
    )
    piv = jnp.where(piv_block < PANEL_BLOCKS, panel_piv, trail_piv)
    pivots = piv.reshape(1, 1, share)
    return (factored, corrected, logdet, pivots)


def solution(mesh):
    in_specs = (P("col", "row", None), P("col", "row"), P(), P())
    out_specs = (
        P(None, "row", None, None, "col", None),
        P(None, "row", None, None, "col", None),
        P(),
        P("row", "col", None),
    )
    return jax.shard_map(body, mesh=mesh, in_specs=in_specs, out_specs=out_specs, check_vma=False)
```
